256 devices in a mesh: rows: 64 (over y, z, core), rhs: 4 (over x).
Axes of the slice: x: 4, y: 4, z: 8, core: 2. Of those that a mesh axis runs over, the one named last changes fastest.
Arguments:
- kernel_rows: bfloat16 [131072, 512], P(('rows', 'rhs')), may hold values from 0 to 1
- factor_blocks: bfloat16 [512, 8, 256, 256], P('rows'), may hold values from -0.125 to 0.125
- diag_inverse: bfloat16 [512, 256, 256], P('rows'), as said below
- pattern: int32 [512, 8], P('rows'), may hold values from 0 to 511, as said below
- live_counts: int32 [512], P('rows'), may hold values from 0 to 8, as said below
Outputs:
- solution: bfloat16 [131072, 512], P('rows', 'rhs')
The draws below stay inside these ranges and needn't reach their ends.
Inputs may be any that keep to these rules, and one draw needn't show every extreme that they name: pattern[s, k] names a block row of a lower level than s; slot 0 of every block row above level 0 names a block row of the level just below; rows of level 0 hold 0. Block row t is held by index t // 8 of rows; the used slots of the block rows held by one index of rows name, for any one level, at most 1 distinct block rows held by any one other index. `live_counts`: 0 on level 0, from 1 to 8 on higher levels, 8 reached. `diag_inverse`: each block is the inverse of a well-conditioned diagonal block of the factor.
All inputs are finite; a program needn't handle non-finite values.
Results may differ from the reference program's by a relative error of at most 0.0058.
Values may be sent and summed in bfloat16 or wider, within the bound.
No kernel may reach another device: no remote copies, remote signals or barrier semaphores. Data moves between devices by JAX's collectives and lax.ppermute only.
A program may use at most 128 MiB of HBM per device.

```python
import jax
import jax.numpy as jnp
import numpy as np
from jax import lax

BLK = 256
RHS = 512
LEV = 4
K = 8
BR_DEV = 2
NB = 512
N_ROWS = 64


def draw_pattern(key, part):
    per_device = LEV * BR_DEV
    total = LEV * BR_DEV * N_ROWS
    block_ids = jnp.arange(total)[:, None]
    level_of = block_ids % per_device // BR_DEV
    first_key, second_key, third_key = jax.random.split(jax.random.fold_in(key, 11), 3)
    picked = jax.random.randint(first_key, (total, K), 0, 420) % jnp.maximum(level_of, 1)
    slot_ids = jnp.arange(K)[None, :]
    source_level = jnp.where(slot_ids == 0, jnp.maximum(level_of - 1, 0), picked)
    orders = jax.random.permutation(second_key, jnp.tile(jnp.arange(N_ROWS)[None, :], (N_ROWS, 1)), axis=1, independent=True)
    owner = block_ids // per_device
    position = (block_ids % per_device * K + slot_ids) % N_ROWS
    source_holder = orders[owner, position]
    source_offset = jax.random.randint(third_key, (total, K), 0, BR_DEV)
    columns = source_holder * per_device + source_level * BR_DEV + source_offset
    return jnp.where(level_of > 0, columns, 0).astype(jnp.int32)


def draw_live_counts(key, part):
    per_device = LEV * BR_DEV
    total = LEV * BR_DEV * N_ROWS
    block_ids = jnp.arange(total)
    level_of = block_ids % per_device // BR_DEV
    counts = 1 + jax.random.randint(jax.random.fold_in(key, 23), (total,), 0, K)
    counts = jnp.where(block_ids == BR_DEV, K, counts)
    return jnp.where(level_of > 0, counts, 0).astype(jnp.int32)


def draw_diag_inverse(key, part):
    total = LEV * BR_DEV * N_ROWS
    first_key, second_key = jax.random.split(jax.random.fold_in(key, 37))
    scales = jax.random.uniform(first_key, (total, BLK), jnp.float32, 0.5, 1.5)
    spread = jax.random.normal(second_key, (total, BLK, BLK), jnp.float32) * (0.35 / BLK ** 0.5)
    eye_mask = jnp.eye(BLK, dtype=jnp.float32)[None, :, :]
    return (spread + eye_mask * scales[:, :, None]).astype(jnp.bfloat16)


def block_scale(key, shape, cuts, low, top_value):
    gain = 1.0
    for dim, blocks in cuts:
        heights = jax.random.uniform(jax.random.fold_in(jax.random.fold_in(key, 6), dim), (blocks,), jnp.float32, low / len(cuts), top_value / len(cuts))
        gain = gain * jnp.repeat(jnp.exp(heights), shape[dim] // blocks).reshape((-1,) + (1,) * (len(shape) - 1 - dim))
    return gain


def noise(own_key, extent, scale, bound, cuts=(), kind=jnp.bfloat16):
    values = jax.random.normal(own_key, extent, jnp.float32) * scale
    if len(cuts) > 0:
        values = block_scale(own_key, extent, cuts, -0.22, 0.18) * values
    return jnp.clip(values, min=-bound, max=bound).astype(kind)


def setup_inputs(seed: int = 0) -> dict:
    arg_keys = jax.random.split(jax.random.key(seed), 6)
    kernel_rows = jnp.clip(1.0 * jax.random.uniform(arg_keys[0], (NB * BLK, RHS), jnp.float32) ** block_scale(arg_keys[0], (NB * BLK, RHS), ((0, 256),), -0.2, 0.2), 0.0, 1.0).astype(jnp.bfloat16)
    factor_blocks = noise(arg_keys[1], (NB, K, BLK, BLK), (K * BLK) ** -0.5, 0.125, ((0, 64),))
    diag_inverse = draw_diag_inverse(jax.random.fold_in(arg_keys[5], 71), 0)
    pattern = draw_pattern(jax.random.fold_in(arg_keys[5], 71), 0)
    live_counts = draw_live_counts(jax.random.fold_in(arg_keys[5], 71), 0)
    return {"kernel_rows": kernel_rows, "factor_blocks": factor_blocks, "diag_inverse": diag_inverse, "pattern": pattern, "live_counts": live_counts}


def reference(kernel_rows, factor_blocks, diag_inverse, pattern, live_counts):
    per_device = LEV * BR_DEV
    right_side = kernel_rows.reshape(NB, BLK, RHS)
    solved = jnp.zeros((NB, BLK, RHS), jnp.bfloat16)
    slot_ids = jnp.arange(K)
    for level_now in range(LEV):
        members = np.array([holder * per_device + level_now * BR_DEV + offset for holder in range(N_ROWS) for offset in range(BR_DEV)], dtype=np.int32)

        def solve_one(member, solved=solved):
            columns = pattern[member]
            active = slot_ids < live_counts[member]
            blocks = jnp.take(solved, columns, axis=0, mode="clip")
            blocks = jnp.where(active[:, None, None], blocks, jnp.zeros_like(blocks))
            summed = jnp.einsum("kij,kjr->ir", factor_blocks[member].astype(jnp.float32), blocks.astype(jnp.float32))
            residual = (right_side[member].astype(jnp.float32) - summed).astype(jnp.bfloat16)
            return jnp.dot(diag_inverse[member], residual, preferred_element_type=jnp.float32).astype(jnp.bfloat16)

        newest = lax.map(solve_one, jnp.asarray(members))
        solved = solved.at[jnp.asarray(members)].set(newest)
    return solved.reshape(NB * BLK, RHS)
```

```python
import jax
import jax.numpy as jnp
import numpy as np
from jax import lax
from jax.sharding import Mesh
from jax.sharding import PartitionSpec as P

LEV = 4
ROWS = ("y", "z", "core")


def ring(n, step):
    return [(i, (i + step) % n) for i in range(n)]


def ring_gather(x, axis, n):
    got = [None] * n
    got[0] = x
    fwd = x
    bwd = x
    for k in range(1, (n - 1) // 2 + 1):
        fwd = lax.ppermute(fwd, axis, ring(n, 1))
        got[n - k] = fwd
        bwd = lax.ppermute(bwd, axis, ring(n, -1))
        got[k] = bwd
    if n % 2 == 0 and n > 1:
        m = fwd.shape[0] // 2
        far_f = lax.ppermute(fwd[:m], axis, ring(n, 1))
        far_b = lax.ppermute(bwd[m:], axis, ring(n, -1))
        got[n // 2] = jnp.concatenate([far_f, far_b], 0)
    return jnp.stack(got)


def gather_level(solved, ny, nz):
    core = lax.axis_index("core")
    other = lax.ppermute(solved, "core", ring(2, 1))
    chip = jnp.where(core == 0, jnp.stack([solved, other]), jnp.stack([other, solved]))
    half = chip.shape[-1] // 2
    part_a = ring_gather(ring_gather(chip[..., :half], "z", nz), "y", ny)
    part_b = ring_gather(ring_gather(chip[..., half:], "y", ny), "z", nz)
    return part_a.reshape(-1, *part_a.shape[-2:]), part_b.reshape(-1, *part_b.shape[-2:])


def make_shards(ny, nz):
    def shards(kernel_rows, factor_blocks, diag_inverse, pattern, live_counts):
        received = lax.all_to_all(kernel_rows, "x", split_axis=1, concat_axis=0, tiled=True)
        per_device = factor_blocks.shape[0]
        slot_count = factor_blocks.shape[1]
        block = factor_blocks.shape[2]
        width = received.shape[1]
        right_side = received.reshape(per_device, block, width)
        per_level = per_device // LEV
        level_of = pattern % per_device // per_level
        holder_of = pattern // per_device
        offset_of = pattern % per_level
        active = jnp.arange(slot_count)[None, :] < live_counts[:, None]
        my_y = lax.axis_index("y")
        my_z = lax.axis_index("z")
        hy = holder_of // (nz * 2)
        hz = holder_of // 2 % nz
        hc = holder_of % 2
        jy = (hy - my_y) % ny
        jz = (hz - my_z) % nz
        index_a = ((jy * nz + jz) * 2 + hc) * per_level + offset_of
        index_b = ((jz * ny + jy) * 2 + hc) * per_level + offset_of
        gathered = []
        solved_all = []
        for level_now in range(LEV):
            lower = level_now * per_level
            upper = lower + per_level
            if level_now == 0:
                summed_now = jnp.zeros((per_level, block, width), jnp.float32)
            else:
                ia = index_a[lower:upper]
                ib = index_b[lower:upper]
                lv = level_of[lower:upper]
                picked = None
                for source, (part_a, part_b) in enumerate(gathered):
                    take_a = jnp.take(part_a, ia, axis=0, mode="clip")
                    take_b = jnp.take(part_b, ib, axis=0, mode="clip")
                    both = jnp.concatenate([take_a, take_b], -1)
                    keep = (lv == source)[:, :, None, None]
                    both = jnp.where(keep, both, jnp.zeros_like(both))
                    picked = both if picked is None else picked + both
                picked = jnp.where(active[lower:upper, :, None, None], picked, jnp.zeros_like(picked))
                summed_now = jnp.einsum(
                    "bkij,bkjr->bir",
                    factor_blocks[lower:upper],
                    picked,
                    preferred_element_type=jnp.float32,
                )
            residual = (right_side[lower:upper].astype(jnp.float32) - summed_now).astype(jnp.bfloat16)
            solved = jnp.einsum(
                "bij,bjr->bir", diag_inverse[lower:upper], residual, preferred_element_type=jnp.float32
            ).astype(jnp.bfloat16)
            solved_all.append(solved)
            if level_now + 1 < LEV:
                gathered.append(gather_level(solved, ny, nz))
        return jnp.concatenate(solved_all, axis=0).reshape(per_device * block, width)

    return shards


def solution(mesh):
    rows = mesh.shape["rows"]
    devices = mesh.devices
    try:
        ny = len({d.coords[1] for d in devices.flat})
        nz = len({d.coords[2] for d in devices.flat})
    except Exception:
        ny, nz = 4, rows // 8
    fine = Mesh(devices.reshape(ny, nz, rows // (ny * nz), mesh.shape["rhs"]), ROWS + ("x",))
    placed = (
        P(ROWS + ("x",), None),
        P(ROWS, None, None, None),
        P(ROWS, None, None),
        P(ROWS, None),
        P(ROWS),
    )
    return jax.shard_map(
        make_shards(ny, nz), mesh=fine, in_specs=placed, out_specs=P(ROWS, "x"), check_vma=False
    )
```

```python
import jax
import jax.numpy as jnp
import numpy as np
from jax import lax
from jax.experimental import pallas as pl
from jax.experimental.pallas import tpu as pltpu
from jax.sharding import Mesh
from jax.sharding import PartitionSpec as P

LEV = 4
ROWS = ("y", "z", "core")


def ring(n, step):
    return [(i, (i + step) % n) for i in range(n)]


def ring_gather(x, axis, n):
    got = [None] * n
    got[0] = x
    fwd = x
    bwd = x
    for k in range(1, (n - 1) // 2 + 1):
        fwd = lax.ppermute(fwd, axis, ring(n, 1))
        got[n - k] = fwd
        bwd = lax.ppermute(bwd, axis, ring(n, -1))
        got[k] = bwd
    if n % 2 == 0 and n > 1:
        m = fwd.shape[0] // 2
        far_f = lax.ppermute(fwd[:m], axis, ring(n, 1))
        far_b = lax.ppermute(bwd[m:], axis, ring(n, -1))
        got[n // 2] = jnp.concatenate([far_f, far_b], 0)
    return jnp.stack(got)


def gather_level(solved, ny, nz):
    core = lax.axis_index("core")
    other = lax.ppermute(solved, "core", ring(2, 1))
    chip = jnp.where(core == 0, jnp.stack([solved, other]), jnp.stack([other, solved]))
    half = chip.shape[-1] // 2
    part_a = ring_gather(ring_gather(chip[..., :half], "z", nz), "y", ny)
    part_b = ring_gather(ring_gather(chip[..., half:], "y", ny), "z", nz)
    return part_a.reshape(-1, *part_a.shape[-2:]), part_b.reshape(-1, *part_b.shape[-2:])


def level_solve(table, factor, right, dinv, sources, slot_count):
    per_level, _, block, _ = factor.shape
    width = right.shape[-1]
    half = sources[0].shape[-1]
    n_src = len(sources) // 2
    total = per_level * slot_count

    def kernel(table_ref, f_ref, r_ref, d_ref, *rest):
        src = rest[: 2 * n_src]
        o_ref, xa, xb, acc, sem = rest[2 * n_src :]
        b = pl.program_id(0)
        slots = []
        for k in range(slot_count):
            ia = table_ref[0 * total + b * slot_count + k]
            ib = table_ref[1 * total + b * slot_count + k]
            lv = table_ref[2 * total + b * slot_count + k]
            act = table_ref[3 * total + b * slot_count + k]
            slots.append((ia, ib, lv, act))
            for level in range(n_src):
                @pl.when((act > 0) & (lv == level))
                def _():
                    pltpu.make_async_copy(src[2 * level].at[ia], xa.at[k], sem.at[0, k]).start()
                    pltpu.make_async_copy(src[2 * level + 1].at[ib], xb.at[k], sem.at[1, k]).start()
        acc[...] = jnp.zeros_like(acc)
        for k in range(slot_count):
            ia, ib, lv, act = slots[k]

            @pl.when((act > 0) & (lv >= 0) & (lv < n_src))
            def _():
                pltpu.make_async_copy(src[0].at[0], xa.at[k], sem.at[0, k]).wait()
                pltpu.make_async_copy(src[1].at[0], xb.at[k], sem.at[1, k]).wait()
                f = f_ref[0, k]
                acc[:, :half] += jnp.dot(f, xa[k], preferred_element_type=jnp.float32)
                acc[:, half:] += jnp.dot(f, xb[k], preferred_element_type=jnp.float32)

        residual = (r_ref[0].astype(jnp.float32) - acc[...]).astype(jnp.bfloat16)
        o_ref[0] = jnp.dot(d_ref[0], residual, preferred_element_type=jnp.float32).astype(o_ref.dtype)

    any_spec = pl.BlockSpec(memory_space=pl.ANY)
    grid_spec = pltpu.PrefetchScalarGridSpec(
        num_scalar_prefetch=1,
        grid=(per_level,),
        in_specs=[
            pl.BlockSpec((1, slot_count, block, block), lambda b, t: (b, 0, 0, 0)),
            pl.BlockSpec((1, block, width), lambda b, t: (b, 0, 0)),
            pl.BlockSpec((1, block, block), lambda b, t: (b, 0, 0)),
        ]
        + [any_spec] * len(sources),
        out_specs=pl.BlockSpec((1, block, width), lambda b, t: (b, 0, 0)),
        scratch_shapes=[
            pltpu.VMEM((slot_count, block, half), sources[0].dtype),
            pltpu.VMEM((slot_count, block, half), sources[0].dtype),
            pltpu.VMEM((block, width), jnp.float32),
            pltpu.SemaphoreType.DMA((2, slot_count)),
        ],
    )
    return pl.pallas_call(
        kernel,
        grid_spec=grid_spec,
        out_shape=jax.ShapeDtypeStruct((per_level, block, width), jnp.bfloat16),
    )(table, factor, right, dinv, *sources)


def make_shards(ny, nz):
    def shards(kernel_rows, factor_blocks, diag_inverse, pattern, live_counts):
        received = lax.all_to_all(kernel_rows, "x", split_axis=1, concat_axis=0, tiled=True)
        per_device = factor_blocks.shape[0]
        slot_count = factor_blocks.shape[1]
        block = factor_blocks.shape[2]
        width = received.shape[1]
        right_side = received.reshape(per_device, block, width)
        per_level = per_device // LEV
        level_of = pattern % per_device // per_level
        holder_of = pattern // per_device
        offset_of = pattern % per_level
        active = jnp.arange(slot_count)[None, :] < live_counts[:, None]
        my_y = lax.axis_index("y")
        my_z = lax.axis_index("z")
        hy = holder_of // (nz * 2)
        hz = holder_of // 2 % nz
        hc = holder_of % 2
        jy = (hy - my_y) % ny
        jz = (hz - my_z) % nz
        index_a = ((jy * nz + jz) * 2 + hc) * per_level + offset_of
        index_b = ((jz * ny + jy) * 2 + hc) * per_level + offset_of
        gathered = []
        solved_all = []
        for level_now in range(LEV):
            lower = level_now * per_level
            upper = lower + per_level
            if level_now == 0:
                residual = right_side[lower:upper]
                solved = jnp.einsum(
                    "bij,bjr->bir", diag_inverse[lower:upper], residual, preferred_element_type=jnp.float32
                ).astype(jnp.bfloat16)
            else:
                n_a = gathered[0][0].shape[0]
                n_b = gathered[0][1].shape[0]
                table = jnp.stack(
                    [
                        jnp.clip(index_a[lower:upper], 0, n_a - 1),
                        jnp.clip(index_b[lower:upper], 0, n_b - 1),
                        level_of[lower:upper],
                        active[lower:upper].astype(jnp.int32),
                    ]
                ).reshape(-1).astype(jnp.int32)
                sources = [part for pair in gathered for part in pair]
                solved = level_solve(
                    table,
                    factor_blocks[lower:upper],
                    right_side[lower:upper],
                    diag_inverse[lower:upper],
                    sources,
                    slot_count,
                )
            solved_all.append(solved)
            if level_now + 1 < LEV:
                gathered.append(gather_level(solved, ny, nz))
        return jnp.concatenate(solved_all, axis=0).reshape(per_device * block, width)

    return shards


def solution(mesh):
    rows = mesh.shape["rows"]
    devices = mesh.devices
    try:
        ny = len({d.coords[1] for d in devices.flat})
        nz = len({d.coords[2] for d in devices.flat})
    except Exception:
        ny, nz = 4, rows // 8
    fine = Mesh(devices.reshape(ny, nz, rows // (ny * nz), mesh.shape["rhs"]), ROWS + ("x",))
    placed = (
        P(ROWS + ("x",), None),
        P(ROWS, None, None, None),
        P(ROWS, None, None),
        P(ROWS, None),
        P(ROWS),
    )
    return jax.shard_map(
        make_shards(ny, nz), mesh=fine, in_specs=placed, out_specs=P(ROWS, "x"), check_vma=False
    )
```

```python
import jax
import jax.numpy as jnp
from jax import lax
from jax.experimental import pallas as pl
from jax.experimental.pallas import tpu as pltpu
from jax.sharding import PartitionSpec as P

LEV = 4


def level_solve(table, factor, right, dinv, sources, slot_count):
    per_level, _, block, _ = factor.shape
    width = right.shape[-1]
    n_src = len(sources)
    total = per_level * slot_count

    def kernel(table_ref, f_ref, r_ref, d_ref, *rest):
        src = rest[:n_src]
        o_ref, xs, acc, sem = rest[n_src:]
        b = pl.program_id(0)
        slots = []
        for k in range(slot_count):
            idx = table_ref[0 * total + b * slot_count + k]
            lv = table_ref[1 * total + b * slot_count + k]
            act = table_ref[2 * total + b * slot_count + k]
            slots.append((idx, lv, act))
            for level in range(n_src):
                @pl.when((act > 0) & (lv == level))
                def _():
                    pltpu.make_async_copy(src[level].at[idx], xs.at[k], sem.at[k]).start()
        acc[...] = jnp.zeros_like(acc)
        for k in range(slot_count):
            idx, lv, act = slots[k]

            @pl.when((act > 0) & (lv >= 0) & (lv < n_src))
            def _():
                pltpu.make_async_copy(src[0].at[0], xs.at[k], sem.at[k]).wait()
                acc[...] += jnp.dot(f_ref[0, k], xs[k], preferred_element_type=jnp.float32)

        residual = (r_ref[0].astype(jnp.float32) - acc[...]).astype(jnp.bfloat16)
        o_ref[0] = jnp.dot(d_ref[0], residual, preferred_element_type=jnp.float32).astype(o_ref.dtype)

    any_spec = pl.BlockSpec(memory_space=pl.ANY)
    grid_spec = pltpu.PrefetchScalarGridSpec(
        num_scalar_prefetch=1,
        grid=(per_level,),
        in_specs=[
            pl.BlockSpec((1, slot_count, block, block), lambda b, t: (b, 0, 0, 0)),
            pl.BlockSpec((1, block, width), lambda b, t: (b, 0, 0)),
            pl.BlockSpec((1, block, block), lambda b, t: (b, 0, 0)),
        ]
        + [any_spec] * n_src,
        out_specs=pl.BlockSpec((1, block, width), lambda b, t: (b, 0, 0)),
        scratch_shapes=[
            pltpu.VMEM((slot_count, block, width), sources[0].dtype),
            pltpu.VMEM((block, width), jnp.float32),
            pltpu.SemaphoreType.DMA((slot_count,)),
        ],
    )
    return pl.pallas_call(
        kernel,
        grid_spec=grid_spec,
        out_shape=jax.ShapeDtypeStruct((per_level, block, width), jnp.bfloat16),
    )(table, factor, right, dinv, *sources)


def shards(kernel_rows, factor_blocks, diag_inverse, pattern, live_counts):
    received = lax.all_to_all(kernel_rows, "rhs", split_axis=1, concat_axis=0, tiled=True)
    per_device = factor_blocks.shape[0]
    slot_count = factor_blocks.shape[1]
    block = factor_blocks.shape[2]
    width = received.shape[1]
    right_side = received.reshape(per_device, block, width)
    holders = lax.axis_size("rows")
    per_level = per_device // LEV
    level_of = pattern % per_device // per_level
    holder_of = pattern // per_device
    offset_of = pattern % per_level
    active = jnp.arange(slot_count)[None, :] < live_counts[:, None]
    position = jnp.clip(holder_of * per_level + offset_of, 0, holders * per_level - 1)
    gathered_all = []
    solved_all = []
    for level_now in range(LEV):
        lower = level_now * per_level
        upper = lower + per_level
        if level_now == 0:
            solved = jnp.einsum(
                "bij,bjr->bir", diag_inverse[lower:upper], right_side[lower:upper],
                preferred_element_type=jnp.float32,
            ).astype(jnp.bfloat16)
        else:
            table = jnp.stack(
                [position[lower:upper], level_of[lower:upper], active[lower:upper].astype(jnp.int32)]
            ).reshape(-1).astype(jnp.int32)
            solved = level_solve(
                table,
                factor_blocks[lower:upper],
                right_side[lower:upper],
                diag_inverse[lower:upper],
                gathered_all,
                slot_count,
            )
        solved_all.append(solved)
        if level_now + 1 < LEV:
            gathered_all.append(lax.all_gather(solved, "rows", axis=0, tiled=True))
    return jnp.concatenate(solved_all, axis=0).reshape(per_device * block, width)


def solution(mesh):
    placed = (
        P(("rows", "rhs"), None),
        P("rows", None, None, None),
        P("rows", None, None),
        P("rows", None),
        P("rows"),
    )
    return jax.shard_map(
        shards, mesh=mesh, in_specs=placed, out_specs=P("rows", "rhs"), check_vma=False
    )
```

```python
import jax
import jax.numpy as jnp
from jax import lax
from jax.experimental import pallas as pl
from jax.experimental.pallas import tpu as pltpu
from jax.sharding import PartitionSpec as P

LEV = 4


def level_solve(table, factor, right, dinv, sources, slot_count):
    per_level, _, block, _ = factor.shape
    width = right.shape[-1]
    n_src = len(sources)
    total = per_level * slot_count

    def kernel(table_ref, f_hbm, r_hbm, d_hbm, *rest):
        src = rest[:n_src]
        o_ref, xs, fs, rs, ds, acc, sem, fsem, rsem = rest[n_src:]
        rcopy = pltpu.make_async_copy(r_hbm, rs, rsem.at[0])
        dcopy = pltpu.make_async_copy(d_hbm, ds, rsem.at[1])
        slots = []
        for s in range(total):
            b, k = divmod(s, slot_count)
            idx = table_ref[0 * total + s]
            lv = table_ref[1 * total + s]
            act = table_ref[2 * total + s]
            used = (act > 0) & (lv >= 0) & (lv < n_src)
            slots.append((used, b, k))
            for level in range(n_src):
                @pl.when((act > 0) & (lv == level))
                def _():
                    pltpu.make_async_copy(src[level].at[idx], xs.at[s], sem.at[s]).start()

            @pl.when(used)
            def _():
                pltpu.make_async_copy(f_hbm.at[b, k], fs.at[s], fsem.at[s]).start()

        rcopy.start()
        dcopy.start()
        rcopy.wait()
        dcopy.wait()
        for b in range(per_level):
            acc[...] = jnp.zeros_like(acc)
            for k in range(slot_count):
                s = b * slot_count + k
                used = slots[s][0]

                @pl.when(used)
                def _():
                    pltpu.make_async_copy(src[0].at[0], xs.at[s], sem.at[s]).wait()
                    pltpu.make_async_copy(f_hbm.at[0, 0], fs.at[s], fsem.at[s]).wait()
                    acc[...] += jnp.dot(fs[s], xs[s], preferred_element_type=jnp.float32)

            residual = (rs[b].astype(jnp.float32) - acc[...]).astype(jnp.bfloat16)
            o_ref[b] = jnp.dot(ds[b], residual, preferred_element_type=jnp.float32).astype(o_ref.dtype)

    any_spec = pl.BlockSpec(memory_space=pl.ANY)
    return pl.pallas_call(
        kernel,
        in_specs=[pl.BlockSpec(memory_space=pltpu.SMEM), any_spec, any_spec, any_spec] + [any_spec] * n_src,
        out_specs=pl.BlockSpec(memory_space=pltpu.VMEM),
        scratch_shapes=[
            pltpu.VMEM((total, block, width), sources[0].dtype),
            pltpu.VMEM((total, block, block), factor.dtype),
            pltpu.VMEM((per_level, block, width), right.dtype),
            pltpu.VMEM((per_level, block, block), dinv.dtype),
            pltpu.VMEM((block, width), jnp.float32),
            pltpu.SemaphoreType.DMA((total,)),
            pltpu.SemaphoreType.DMA((total,)),
            pltpu.SemaphoreType.DMA((2,)),
        ],
        out_shape=jax.ShapeDtypeStruct((per_level, block, width), jnp.bfloat16),
    )(table, factor, right, dinv, *sources)


def shards(kernel_rows, factor_blocks, diag_inverse, pattern, live_counts):
    received = lax.all_to_all(kernel_rows, "rhs", split_axis=1, concat_axis=0, tiled=True)
    per_device = factor_blocks.shape[0]
    slot_count = factor_blocks.shape[1]
    block = factor_blocks.shape[2]
    width = received.shape[1]
    right_side = received.reshape(per_device, block, width)
    holders = lax.axis_size("rows")
    per_level = per_device // LEV
    level_of = pattern % per_device // per_level
    holder_of = pattern // per_device
    offset_of = pattern % per_level
    active = jnp.arange(slot_count)[None, :] < live_counts[:, None]
    position = jnp.clip(holder_of * per_level + offset_of, 0, holders * per_level - 1)
    gathered_all = []
    solved_all = []
    for level_now in range(LEV):
        lower = level_now * per_level
        upper = lower + per_level
        if level_now == 0:
            solved = jnp.einsum(
                "bij,bjr->bir", diag_inverse[lower:upper], right_side[lower:upper],
                preferred_element_type=jnp.float32,
            ).astype(jnp.bfloat16)
        else:
            table = jnp.stack(
                [position[lower:upper], level_of[lower:upper], active[lower:upper].astype(jnp.int32)]
            ).reshape(-1).astype(jnp.int32)
            solved = level_solve(
                table,
                factor_blocks[lower:upper],
                right_side[lower:upper],
                diag_inverse[lower:upper],
                gathered_all,
                slot_count,
            )
        solved_all.append(solved)
        if level_now + 1 < LEV:
            gathered_all.append(lax.all_gather(solved, "rows", axis=0, tiled=True))
    return jnp.concatenate(solved_all, axis=0).reshape(per_device * block, width)


def solution(mesh):
    placed = (
        P(("rows", "rhs"), None),
        P("rows", None, None, None),
        P("rows", None, None),
        P("rows", None),
        P("rows"),
    )
    return jax.shard_map(
        shards, mesh=mesh, in_specs=placed, out_specs=P("rows", "rhs"), check_vma=False
    )
```

```python
import jax
import jax.numpy as jnp
from jax import lax
from jax.experimental import pallas as pl
from jax.experimental.pallas import tpu as pltpu
from jax.sharding import Mesh
from jax.sharding import PartitionSpec as P

LEV = 4
ROWS = ("y", "z", "core")


def ring(n, step):
    return [(i, (i + step) % n) for i in range(n)]


def ring_pieces(x, axis, n):
    lead = x.shape[0]
    pieces = [(x, 0, 0, lead)]
    fwd = x
    bwd = x
    for k in range(1, (n - 1) // 2 + 1):
        fwd = lax.ppermute(fwd, axis, ring(n, 1))
        pieces.append((fwd, n - k, 0, lead))
        bwd = lax.ppermute(bwd, axis, ring(n, -1))
        pieces.append((bwd, k, 0, lead))
    if n % 2 == 0 and n > 1:
        m = lead // 2
        pieces.append((lax.ppermute(fwd[:m], axis, ring(n, 1)), n // 2, 0, m))
        pieces.append((lax.ppermute(bwd[m:], axis, ring(n, -1)), n // 2, m, lead - m))
    return pieces


def ring_stack(x, axis, n):
    got = [None] * n
    for arr, j, lo, count in ring_pieces(x, axis, n):
        got[j] = arr if got[j] is None else jnp.concatenate([got[j], arr], 0)
    return jnp.stack(got)


def gather_level(solved, ny, nz):
    core = lax.axis_index("core")
    other = lax.ppermute(solved, "core", ring(2, 1))
    chip = jnp.where(core == 0, jnp.stack([solved, other]), jnp.stack([other, solved]))
    out = []
    by_z = ring_stack(chip[:, 0], "z", nz)
    for arr, j, lo, count in ring_pieces(by_z, "y", ny):
        out.append((arr.reshape(-1, *arr.shape[-2:]), 0, j, lo, count))
    by_y = ring_stack(chip[:, 1], "y", ny)
    for arr, j, lo, count in ring_pieces(by_y, "z", nz):
        out.append((arr.reshape(-1, *arr.shape[-2:]), 1, j, lo, count))
    return out


def level_solve(table, factor, right, dinv, sources, slot_count):
    per_level, _, block, _ = factor.shape
    width = right.shape[-1]
    n_src = len(sources)
    total = per_level * slot_count

    def kernel(table_ref, f_hbm, r_hbm, d_hbm, *rest):
        src = rest[:n_src]
        o_ref, xs, fs, rs, ds, acc, sem, fsem, rsem = rest[n_src:]
        rcopy = pltpu.make_async_copy(r_hbm, rs, rsem.at[0])
        dcopy = pltpu.make_async_copy(d_hbm, ds, rsem.at[1])
        slots = []
        for s in range(total):
            b, k = divmod(s, slot_count)
            idx = table_ref[0 * total + s]
            piece = table_ref[1 * total + s]
            act = table_ref[2 * total + s]
            used = (act > 0) & (piece >= 0) & (piece < n_src)
            slots.append((used, b, k))
            for p in range(n_src):
                @pl.when((act > 0) & (piece == p))
                def _():
                    pltpu.make_async_copy(src[p].at[idx], xs.at[s], sem.at[s]).start()

            @pl.when(used)
            def _():
                pltpu.make_async_copy(f_hbm.at[b, k], fs.at[s], fsem.at[s]).start()

        rcopy.start()
        dcopy.start()
        rcopy.wait()
        dcopy.wait()
        for b in range(per_level):
            acc[...] = jnp.zeros_like(acc)
            for k in range(slot_count):
                s = b * slot_count + k
                used = slots[s][0]

                @pl.when(used)
                def _():
                    pltpu.make_async_copy(src[0].at[0], xs.at[s], sem.at[s]).wait()
                    pltpu.make_async_copy(f_hbm.at[0, 0], fs.at[s], fsem.at[s]).wait()
                    acc[...] += jnp.dot(fs[s], xs[s], preferred_element_type=jnp.float32)

            residual = (rs[b].astype(jnp.float32) - acc[...]).astype(jnp.bfloat16)
            o_ref[b] = jnp.dot(ds[b], residual, preferred_element_type=jnp.float32).astype(o_ref.dtype)

    any_spec = pl.BlockSpec(memory_space=pl.ANY)
    return pl.pallas_call(
        kernel,
        in_specs=[pl.BlockSpec(memory_space=pltpu.SMEM), any_spec, any_spec, any_spec] + [any_spec] * n_src,
        out_specs=pl.BlockSpec(memory_space=pltpu.VMEM),
        scratch_shapes=[
            pltpu.VMEM((total, block, width), right.dtype),
            pltpu.VMEM((total, block, block), factor.dtype),
            pltpu.VMEM((per_level, block, width), right.dtype),
            pltpu.VMEM((per_level, block, block), dinv.dtype),
            pltpu.VMEM((block, width), jnp.float32),
            pltpu.SemaphoreType.DMA((total,)),
            pltpu.SemaphoreType.DMA((total,)),
            pltpu.SemaphoreType.DMA((2,)),
        ],
        out_shape=jax.ShapeDtypeStruct((per_level, block, width), jnp.bfloat16),
    )(table, factor, right, dinv, *sources)


def make_shards(ny, nz):
    def shards(kernel_rows, factor_blocks, diag_inverse, pattern, live_counts):
        received = lax.all_to_all(kernel_rows, "x", split_axis=1, concat_axis=0, tiled=True)
        per_device = factor_blocks.shape[0]
        slot_count = factor_blocks.shape[1]
        block = factor_blocks.shape[2]
        width = received.shape[1]
        right_side = received.reshape(per_device, block, width)
        per_level = per_device // LEV
        level_of = pattern % per_device // per_level
        holder_of = pattern // per_device
        offset_of = pattern % per_level
        active = (jnp.arange(slot_count)[None, :] < live_counts[:, None]).astype(jnp.int32)
        hc = holder_of % 2
        jy = (holder_of // (nz * 2) - lax.axis_index("y")) % ny
        jz = (holder_of // 2 % nz - lax.axis_index("z")) % nz
        pieces = []
        solved_all = []
        for level_now in range(LEV):
            lower = level_now * per_level
            upper = lower + per_level
            if level_now == 0:
                solved = jnp.einsum(
                    "bij,bjr->bir", diag_inverse[lower:upper], right_side[lower:upper],
                    preferred_element_type=jnp.float32,
                ).astype(jnp.bfloat16)
            else:
                lv = level_of[lower:upper]
                off = offset_of[lower:upper]
                sy = jy[lower:upper]
                sz = jz[lower:upper]
                sc = hc[lower:upper]
                piece_id = jnp.full(lv.shape, -1, jnp.int32)
                local = jnp.zeros(lv.shape, jnp.int32)
                for p, (source, (arr, kind, j, lo, count)) in enumerate(pieces):
                    main, sub = (sy, sz) if kind == 0 else (sz, sy)
                    match = (lv == source) & (off == kind) & (main == j) & (sub >= lo) & (sub < lo + count)
                    piece_id = jnp.where(match, p, piece_id)
                    local = jnp.where(match, (sub - lo) * 2 + sc, local)
                table = jnp.stack([local, piece_id, active[lower:upper]]).reshape(-1).astype(jnp.int32)
                solved = level_solve(
                    table,
                    factor_blocks[lower:upper],
                    right_side[lower:upper],
                    diag_inverse[lower:upper],
                    [arr for _, (arr, *_rest) in pieces],
                    slot_count,
                )
            solved_all.append(solved)
            if level_now + 1 < LEV:
                pieces += [(level_now, piece) for piece in gather_level(solved, ny, nz)]
        return jnp.concatenate(solved_all, axis=0).reshape(per_device * block, width)

    return shards


def solution(mesh):
    rows = mesh.shape["rows"]
    devices = mesh.devices
    try:
        ny = len({d.coords[1] for d in devices.flat})
        nz = len({d.coords[2] for d in devices.flat})
    except Exception:
        ny, nz = 4, rows // 8
    fine = Mesh(devices.reshape(ny, nz, rows // (ny * nz), mesh.shape["rhs"]), ROWS + ("x",))
    placed = (
        P(ROWS + ("x",), None),
        P(ROWS, None, None, None),
        P(ROWS, None, None),
        P(ROWS, None),
        P(ROWS),
    )
    return jax.shard_map(
        make_shards(ny, nz), mesh=fine, in_specs=placed, out_specs=P(ROWS, "x"), check_vma=False
    )
```

```python
import jax
import jax.numpy as jnp
from jax import lax
from jax.experimental import pallas as pl
from jax.experimental.pallas import tpu as pltpu
from jax.sharding import PartitionSpec as P

LEV = 4


def level_solve(table, factor, right, dinv, sources, slot_count, earlier=()):
    per_level, _, block, _ = factor.shape
    width = right.shape[-1]
    n_src = len(sources)
    n_early = len(earlier)
    total = per_level * slot_count

    def kernel(table_ref, f_hbm, r_hbm, d_hbm, *rest):
        src = rest[:n_src]
        early = rest[n_src : n_src + n_early]
        o_ref, xs, fs, rs, ds, acc, sem, fsem, rsem, esem = rest[n_src + n_early :]
        done = per_level * n_early
        ecopies = [
            pltpu.make_async_copy(e, o_ref.at[pl.ds(i * per_level, per_level)], esem.at[i])
            for i, e in enumerate(early)
        ]
        for c in ecopies:
            c.start()
        rcopy = pltpu.make_async_copy(r_hbm, rs, rsem.at[0])
        dcopy = pltpu.make_async_copy(d_hbm, ds, rsem.at[1])
        slots = []
        for s in range(total):
            b, k = divmod(s, slot_count)
            idx = table_ref[0 * total + s]
            lv = table_ref[1 * total + s]
            act = table_ref[2 * total + s]
            used = (act > 0) & (lv >= 0) & (lv < n_src)
            slots.append((used, b, k))
            for level in range(n_src):
                @pl.when((act > 0) & (lv == level))
                def _():
                    pltpu.make_async_copy(src[level].at[idx], xs.at[s], sem.at[s]).start()

            @pl.when(used)
            def _():
                pltpu.make_async_copy(f_hbm.at[b, k], fs.at[s], fsem.at[s]).start()

        rcopy.start()
        dcopy.start()
        rcopy.wait()
        dcopy.wait()
        for c in ecopies:
            c.wait()
        for b in range(per_level):
            acc[...] = jnp.zeros_like(acc)
            for k in range(slot_count):
                s = b * slot_count + k
                used = slots[s][0]

                @pl.when(used)
                def _():
                    pltpu.make_async_copy(src[0].at[0], xs.at[s], sem.at[s]).wait()
                    pltpu.make_async_copy(f_hbm.at[0, 0], fs.at[s], fsem.at[s]).wait()
                    acc[...] += jnp.dot(fs[s], xs[s], preferred_element_type=jnp.float32)

            residual = (rs[b].astype(jnp.float32) - acc[...]).astype(jnp.bfloat16)
            o_ref[done + b] = jnp.dot(ds[b], residual, preferred_element_type=jnp.float32).astype(o_ref.dtype)

    any_spec = pl.BlockSpec(memory_space=pl.ANY)
    return pl.pallas_call(
        kernel,
        in_specs=[pl.BlockSpec(memory_space=pltpu.SMEM), any_spec, any_spec, any_spec]
        + [any_spec] * (n_src + n_early),
        out_specs=pl.BlockSpec(memory_space=pltpu.VMEM),
        scratch_shapes=[
            pltpu.VMEM((total, block, width), sources[0].dtype),
            pltpu.VMEM((total, block, block), factor.dtype),
            pltpu.VMEM((per_level, block, width), right.dtype),
            pltpu.VMEM((per_level, block, block), dinv.dtype),
            pltpu.VMEM((block, width), jnp.float32),
            pltpu.SemaphoreType.DMA((total,)),
            pltpu.SemaphoreType.DMA((total,)),
            pltpu.SemaphoreType.DMA((2,)),
            pltpu.SemaphoreType.DMA((max(n_early, 1),)),
        ],
        out_shape=jax.ShapeDtypeStruct((per_level * (n_early + 1), block, width), jnp.bfloat16),
    )(table, factor, right, dinv, *sources, *earlier)


def shards(kernel_rows, factor_blocks, diag_inverse, pattern, live_counts):
    received = lax.all_to_all(kernel_rows, "rhs", split_axis=1, concat_axis=0, tiled=True)
    per_device = factor_blocks.shape[0]
    slot_count = factor_blocks.shape[1]
    block = factor_blocks.shape[2]
    width = received.shape[1]
    right_side = received.reshape(per_device, block, width)
    holders = lax.axis_size("rows")
    per_level = per_device // LEV
    level_of = pattern % per_device // per_level
    holder_of = pattern // per_device
    offset_of = pattern % per_level
    active = jnp.arange(slot_count)[None, :] < live_counts[:, None]
    position = jnp.clip(holder_of * per_level + offset_of, 0, holders * per_level - 1)
    gathered_all = []
    solved_all = []
    for level_now in range(LEV):
        lower = level_now * per_level
        upper = lower + per_level
        if level_now == 0:
            solved = jnp.einsum(
                "bij,bjr->bir", diag_inverse[lower:upper], right_side[lower:upper],
                preferred_element_type=jnp.float32,
            ).astype(jnp.bfloat16)
        else:
            table = jnp.stack(
                [position[lower:upper], level_of[lower:upper], active[lower:upper].astype(jnp.int32)]
            ).reshape(-1).astype(jnp.int32)
            solved = level_solve(
                table,
                factor_blocks[lower:upper],
                right_side[lower:upper],
                diag_inverse[lower:upper],
                gathered_all,
                slot_count,
                earlier=tuple(solved_all) if level_now + 1 == LEV else (),
            )
        if level_now + 1 < LEV:
            solved_all.append(solved)
            gathered_all.append(lax.all_gather(solved, "rows", axis=0, tiled=True))
    return solved.reshape(per_device * block, width)


def solution(mesh):
    placed = (
        P(("rows", "rhs"), None),
        P("rows", None, None, None),
        P("rows", None, None),
        P("rows", None),
        P("rows"),
    )
    return jax.shard_map(
        shards, mesh=mesh, in_specs=placed, out_specs=P("rows", "rhs"), check_vma=False
    )
```

```python
import jax
import jax.numpy as jnp
from jax import lax
from jax.experimental import pallas as pl
from jax.experimental.pallas import tpu as pltpu
from jax.sharding import PartitionSpec as P

LEV = 4


def level_solve(table, factor, right, dinv, sources, slot_count, earlier=(), init=None):
    per_level, _, block, _ = factor.shape
    width = right.shape[-1]
    n_src = len(sources)
    n_early = len(earlier)
    n_init = 0 if init is None else 1
    total = per_level * slot_count

    def kernel(table_ref, f_hbm, r_hbm, d_hbm, *rest):
        src = rest[:n_src]
        early = rest[n_src : n_src + n_early]
        start_ref = rest[n_src + n_early : n_src + n_early + n_init]
        o_ref, xs, fs, rs, ds, acc, ini, sem, fsem, rsem, esem = rest[n_src + n_early + n_init :]
        icopies = [pltpu.make_async_copy(r, ini, rsem.at[2]) for r in start_ref]
        for c in icopies:
            c.start()
        done = per_level * n_early
        ecopies = [
            pltpu.make_async_copy(e, o_ref.at[pl.ds(i * per_level, per_level)], esem.at[i])
            for i, e in enumerate(early)
        ]
        for c in ecopies:
            c.start()
        rcopy = pltpu.make_async_copy(r_hbm, rs, rsem.at[0])
        dcopy = pltpu.make_async_copy(d_hbm, ds, rsem.at[1])
        slots = []
        for s in range(total):
            b, k = divmod(s, slot_count)
            idx = table_ref[0 * total + s]
            lv = table_ref[1 * total + s]
            act = table_ref[2 * total + s]
            used = (act > 0) & (lv >= 0) & (lv < n_src)
            slots.append((used, b, k))
            for level in range(n_src):
                @pl.when((act > 0) & (lv == level))
                def _():
                    pltpu.make_async_copy(src[level].at[idx], xs.at[s], sem.at[s]).start()

            @pl.when(used)
            def _():
                pltpu.make_async_copy(f_hbm.at[b, k], fs.at[s], fsem.at[s]).start()

        rcopy.start()
        dcopy.start()
        rcopy.wait()
        dcopy.wait()
        for c in ecopies:
            c.wait()
        for c in icopies:
            c.wait()
        for b in range(per_level):
            if n_init:
                acc[...] = ini[b]
            else:
                acc[...] = jnp.zeros_like(acc)
            for k in range(slot_count):
                s = b * slot_count + k
                used = slots[s][0]

                @pl.when(used)
                def _():
                    pltpu.make_async_copy(src[0].at[0], xs.at[s], sem.at[s]).wait()
                    pltpu.make_async_copy(f_hbm.at[0, 0], fs.at[s], fsem.at[s]).wait()
                    acc[...] += jnp.dot(fs[s], xs[s], preferred_element_type=jnp.float32)

            residual = (rs[b].astype(jnp.float32) - acc[...]).astype(jnp.bfloat16)
            o_ref[done + b] = jnp.dot(ds[b], residual, preferred_element_type=jnp.float32).astype(o_ref.dtype)

    any_spec = pl.BlockSpec(memory_space=pl.ANY)
    return pl.pallas_call(
        kernel,
        in_specs=[pl.BlockSpec(memory_space=pltpu.SMEM), any_spec, any_spec, any_spec]
        + [any_spec] * (n_src + n_early + n_init),
        out_specs=pl.BlockSpec(memory_space=pltpu.VMEM),
        scratch_shapes=[
            pltpu.VMEM((total, block, width), sources[0].dtype),
            pltpu.VMEM((total, block, block), factor.dtype),
            pltpu.VMEM((per_level, block, width), right.dtype),
            pltpu.VMEM((per_level, block, block), dinv.dtype),
            pltpu.VMEM((block, width), jnp.float32),
            pltpu.VMEM((per_level, block, width), jnp.float32),
            pltpu.SemaphoreType.DMA((total,)),
            pltpu.SemaphoreType.DMA((total,)),
            pltpu.SemaphoreType.DMA((3,)),
            pltpu.SemaphoreType.DMA((max(n_early, 1),)),
        ],
        out_shape=jax.ShapeDtypeStruct((per_level * (n_early + 1), block, width), jnp.bfloat16),
    )(table, factor, right, dinv, *sources, *earlier, *([] if init is None else [init]))


def partial_sum(table, factor, sources, slot_count, width):
    per_level, _, block, _ = factor.shape
    n_src = len(sources)
    total = per_level * slot_count

    def kernel(table_ref, f_hbm, *rest):
        src = rest[:n_src]
        o_ref, xs, fs, sem, fsem = rest[n_src:]
        slots = []
        for s in range(total):
            b, k = divmod(s, slot_count)
            idx = table_ref[0 * total + s]
            lv = table_ref[1 * total + s]
            act = table_ref[2 * total + s]
            used = (act > 0) & (lv >= 0) & (lv < n_src)
            slots.append(used)
            for level in range(n_src):
                @pl.when((act > 0) & (lv == level))
                def _():
                    pltpu.make_async_copy(src[level].at[idx], xs.at[s], sem.at[s]).start()

            @pl.when(used)
            def _():
                pltpu.make_async_copy(f_hbm.at[b, k], fs.at[s], fsem.at[s]).start()

        for b in range(per_level):
            o_ref[b] = jnp.zeros((block, width), jnp.float32)
            for k in range(slot_count):
                s = b * slot_count + k

                @pl.when(slots[s])
                def _():
                    pltpu.make_async_copy(src[0].at[0], xs.at[s], sem.at[s]).wait()
                    pltpu.make_async_copy(f_hbm.at[0, 0], fs.at[s], fsem.at[s]).wait()
                    o_ref[b] += jnp.dot(fs[s], xs[s], preferred_element_type=jnp.float32)

    any_spec = pl.BlockSpec(memory_space=pl.ANY)
    return pl.pallas_call(
        kernel,
        in_specs=[pl.BlockSpec(memory_space=pltpu.SMEM), any_spec] + [any_spec] * n_src,
        out_specs=pl.BlockSpec(memory_space=pltpu.VMEM),
        scratch_shapes=[
            pltpu.VMEM((total, block, width), sources[0].dtype),
            pltpu.VMEM((total, block, block), factor.dtype),
            pltpu.SemaphoreType.DMA((total,)),
            pltpu.SemaphoreType.DMA((total,)),
        ],
        out_shape=jax.ShapeDtypeStruct((per_level, block, width), jnp.float32),
    )(table, factor, *sources)


def shards(kernel_rows, factor_blocks, diag_inverse, pattern, live_counts):
    received = lax.all_to_all(kernel_rows, "rhs", split_axis=1, concat_axis=0, tiled=True)
    per_device = factor_blocks.shape[0]
    slot_count = factor_blocks.shape[1]
    block = factor_blocks.shape[2]
    width = received.shape[1]
    right_side = received.reshape(per_device, block, width)
    holders = lax.axis_size("rows")
    per_level = per_device // LEV
    level_of = pattern % per_device // per_level
    holder_of = pattern // per_device
    offset_of = pattern % per_level
    active = jnp.arange(slot_count)[None, :] < live_counts[:, None]
    position = jnp.clip(holder_of * per_level + offset_of, 0, holders * per_level - 1)
    gathered_all = []
    solved_all = []
    for level_now in range(LEV):
        lower = level_now * per_level
        upper = lower + per_level
        if level_now == 0:
            solved = jnp.einsum(
                "bij,bjr->bir", diag_inverse[lower:upper], right_side[lower:upper],
                preferred_element_type=jnp.float32,
            ).astype(jnp.bfloat16)
        else:
            newest = level_now - 1
            pos = position[lower:upper]
            lv = level_of[lower:upper]
            act = active[lower:upper].astype(jnp.int32)
            init = None
            if newest > 0:
                old_table = jnp.stack([pos, lv, act]).reshape(-1).astype(jnp.int32)
                init = partial_sum(old_table, factor_blocks[lower:upper], gathered_all[:newest], slot_count, width)
            table = jnp.stack([pos, jnp.where(lv == newest, 0, -1), act]).reshape(-1).astype(jnp.int32)
            solved = level_solve(
                table,
                factor_blocks[lower:upper],
                right_side[lower:upper],
                diag_inverse[lower:upper],
                gathered_all[newest:],
                slot_count,
                earlier=tuple(solved_all) if level_now + 1 == LEV else (),
                init=init,
            )
        if level_now + 1 < LEV:
            solved_all.append(solved)
            gathered_all.append(lax.all_gather(solved, "rows", axis=0, tiled=True))
    return solved.reshape(per_device * block, width)


def solution(mesh):
    placed = (
        P(("rows", "rhs"), None),
        P("rows", None, None, None),
        P("rows", None, None),
        P("rows", None),
        P("rows"),
    )
    return jax.shard_map(
        shards, mesh=mesh, in_specs=placed, out_specs=P("rows", "rhs"), check_vma=False
    )
```

```python
import jax
import jax.numpy as jnp
from jax import lax
from jax.experimental import pallas as pl
from jax.experimental.pallas import tpu as pltpu
from jax.sharding import PartitionSpec as P

LEV = 4


def level_solve(table, factor, right, dinv, sources, slot_count, earlier=(), init=None):
    per_level, _, block, _ = factor.shape
    width = right.shape[-1]
    n_src = len(sources)
    n_early = len(earlier)
    n_init = 0 if init is None else 1
    total = per_level * slot_count

    def kernel(table_ref, f_hbm, r_hbm, d_hbm, *rest):
        src = rest[:n_src]
        early = rest[n_src : n_src + n_early]
        start_ref = rest[n_src + n_early : n_src + n_early + n_init]
        o_ref, xs, fs, rs, ds, acc, ini, sem, fsem, rsem, esem = rest[n_src + n_early + n_init :]
        icopies = [pltpu.make_async_copy(r, ini, rsem.at[2]) for r in start_ref]
        for c in icopies:
            c.start()
        rcopy = pltpu.make_async_copy(r_hbm, rs, rsem.at[0])
        dcopy = pltpu.make_async_copy(d_hbm, ds, rsem.at[1])
        rcopy.start()
        dcopy.start()
        done = per_level * n_early
        ecopies = [
            pltpu.make_async_copy(e, o_ref.at[pl.ds(i * per_level, per_level)], esem.at[i])
            for i, e in enumerate(early)
        ]
        for c in ecopies:
            c.start()
        slots = []
        for s in range(total):
            b, k = divmod(s, slot_count)
            idx = table_ref[0 * total + s]
            lv = table_ref[1 * total + s]
            act = table_ref[2 * total + s]
            used = (act > 0) & (lv >= 0) & (lv < n_src)
            slots.append((used, b, k))
            for level in range(n_src):
                @pl.when((act > 0) & (lv == level))
                def _():
                    pltpu.make_async_copy(src[level].at[idx], xs.at[s], sem.at[s]).start()

            @pl.when(used)
            def _():
                pltpu.make_async_copy(f_hbm.at[b, k], fs.at[s], fsem.at[s]).start()

        for c in icopies:
            c.wait()
        for b in range(per_level):
            if n_init:
                acc[...] = ini[b]
            else:
                acc[...] = jnp.zeros_like(acc)
            for k in range(slot_count):
                s = b * slot_count + k
                used = slots[s][0]

                @pl.when(used)
                def _():
                    pltpu.make_async_copy(src[0].at[0], xs.at[s], sem.at[s]).wait()
                    pltpu.make_async_copy(f_hbm.at[0, 0], fs.at[s], fsem.at[s]).wait()
                    acc[...] += jnp.dot(fs[s], xs[s], preferred_element_type=jnp.float32)

            if b == 0:
                rcopy.wait()
                dcopy.wait()
                for c in ecopies:
                    c.wait()
            residual = (rs[b].astype(jnp.float32) - acc[...]).astype(jnp.bfloat16)
            o_ref[done + b] = jnp.dot(ds[b], residual, preferred_element_type=jnp.float32).astype(o_ref.dtype)

    any_spec = pl.BlockSpec(memory_space=pl.ANY)
    return pl.pallas_call(
        kernel,
        in_specs=[pl.BlockSpec(memory_space=pltpu.SMEM), any_spec, any_spec, any_spec]
        + [any_spec] * (n_src + n_early + n_init),
        out_specs=pl.BlockSpec(memory_space=pltpu.VMEM),
        scratch_shapes=[
            pltpu.VMEM((total, block, width), sources[0].dtype),
            pltpu.VMEM((total, block, block), factor.dtype),
            pltpu.VMEM((per_level, block, width), right.dtype),
            pltpu.VMEM((per_level, block, block), dinv.dtype),
            pltpu.VMEM((block, width), jnp.float32),
            pltpu.VMEM((per_level, block, width), jnp.float32),
            pltpu.SemaphoreType.DMA((total,)),
            pltpu.SemaphoreType.DMA((total,)),
            pltpu.SemaphoreType.DMA((3,)),
            pltpu.SemaphoreType.DMA((max(n_early, 1),)),
        ],
        out_shape=jax.ShapeDtypeStruct((per_level * (n_early + 1), block, width), jnp.bfloat16),
    )(table, factor, right, dinv, *sources, *earlier, *([] if init is None else [init]))


def partial_sum(table, factor, sources, slot_count, width):
    per_level, _, block, _ = factor.shape
    n_src = len(sources)
    total = per_level * slot_count

    def kernel(table_ref, f_hbm, *rest):
        src = rest[:n_src]
        o_ref, xs, fs, sem, fsem = rest[n_src:]
        slots = []
        for s in range(total):
            b, k = divmod(s, slot_count)
            idx = table_ref[0 * total + s]
            lv = table_ref[1 * total + s]
            act = table_ref[2 * total + s]
            used = (act > 0) & (lv >= 0) & (lv < n_src)
            slots.append(used)
            for level in range(n_src):
                @pl.when((act > 0) & (lv == level))
                def _():
                    pltpu.make_async_copy(src[level].at[idx], xs.at[s], sem.at[s]).start()

            @pl.when(used)
            def _():
                pltpu.make_async_copy(f_hbm.at[b, k], fs.at[s], fsem.at[s]).start()

        for b in range(per_level):
            o_ref[b] = jnp.zeros((block, width), jnp.float32)
            for k in range(slot_count):
                s = b * slot_count + k

                @pl.when(slots[s])
                def _():
                    pltpu.make_async_copy(src[0].at[0], xs.at[s], sem.at[s]).wait()
                    pltpu.make_async_copy(f_hbm.at[0, 0], fs.at[s], fsem.at[s]).wait()
                    o_ref[b] += jnp.dot(fs[s], xs[s], preferred_element_type=jnp.float32)

    any_spec = pl.BlockSpec(memory_space=pl.ANY)
    return pl.pallas_call(
        kernel,
        in_specs=[pl.BlockSpec(memory_space=pltpu.SMEM), any_spec] + [any_spec] * n_src,
        out_specs=pl.BlockSpec(memory_space=pltpu.VMEM),
        scratch_shapes=[
            pltpu.VMEM((total, block, width), sources[0].dtype),
            pltpu.VMEM((total, block, block), factor.dtype),
            pltpu.SemaphoreType.DMA((total,)),
            pltpu.SemaphoreType.DMA((total,)),
        ],
        out_shape=jax.ShapeDtypeStruct((per_level, block, width), jnp.float32),
    )(table, factor, *sources)


def shards(kernel_rows, factor_blocks, diag_inverse, pattern, live_counts):
    received = lax.all_to_all(kernel_rows, "rhs", split_axis=1, concat_axis=0, tiled=True)
    per_device = factor_blocks.shape[0]
    slot_count = factor_blocks.shape[1]
    block = factor_blocks.shape[2]
    width = received.shape[1]
    right_side = received.reshape(per_device, block, width)
    holders = lax.axis_size("rows")
    per_level = per_device // LEV
    level_of = pattern % per_device // per_level
    holder_of = pattern // per_device
    offset_of = pattern % per_level
    active = jnp.arange(slot_count)[None, :] < live_counts[:, None]
    position = jnp.clip(holder_of * per_level + offset_of, 0, holders * per_level - 1)
    gathered_all = []
    solved_all = []
    for level_now in range(LEV):
        lower = level_now * per_level
        upper = lower + per_level
        if level_now == 0:
            solved = jnp.einsum(
                "bij,bjr->bir", diag_inverse[lower:upper], right_side[lower:upper],
                preferred_element_type=jnp.float32,
            ).astype(jnp.bfloat16)
        else:
            newest = level_now - 1
            pos = position[lower:upper]
            lv = level_of[lower:upper]
            act = active[lower:upper].astype(jnp.int32)
            init = None
            if newest > 0:
                old_table = jnp.stack([pos, lv, act]).reshape(-1).astype(jnp.int32)
                init = partial_sum(old_table, factor_blocks[lower:upper], gathered_all[:newest], slot_count, width)
            table = jnp.stack([pos, jnp.where(lv == newest, 0, -1), act]).reshape(-1).astype(jnp.int32)
            solved = level_solve(
                table,
                factor_blocks[lower:upper],
                right_side[lower:upper],
                diag_inverse[lower:upper],
                gathered_all[newest:],
                slot_count,
                earlier=tuple(solved_all) if level_now + 1 == LEV else (),
                init=init,
            )
        if level_now + 1 < LEV:
            solved_all.append(solved)
            gathered_all.append(lax.all_gather(solved, "rows", axis=0, tiled=True))
    return solved.reshape(per_device * block, width)


def solution(mesh):
    placed = (
        P(("rows", "rhs"), None),
        P("rows", None, None, None),
        P("rows", None, None),
        P("rows", None),
        P("rows"),
    )
    return jax.shard_map(
        shards, mesh=mesh, in_specs=placed, out_specs=P("rows", "rhs"), check_vma=False
    )
```

```python
import jax
import jax.numpy as jnp
from jax import lax
from jax.experimental import pallas as pl
from jax.experimental.pallas import tpu as pltpu
from jax.sharding import PartitionSpec as P

LEV = 4


def level_solve(table, factor, right, dinv, sources, slot_count, base, per_level, earlier=(), init=None):
    block = factor.shape[2]
    width = right.shape[-1]
    n_src = len(sources)
    n_early = len(earlier)
    n_init = 0 if init is None else 1
    total = per_level * slot_count

    def kernel(table_ref, f_hbm, r_hbm, d_hbm, *rest):
        src = rest[:n_src]
        early = rest[n_src : n_src + n_early]
        start_ref = rest[n_src + n_early : n_src + n_early + n_init]
        o_ref, xs, fs, rs, ds, acc, ini, sem, fsem, rsem, esem = rest[n_src + n_early + n_init :]
        icopies = [pltpu.make_async_copy(r, ini, rsem.at[2]) for r in start_ref]
        for c in icopies:
            c.start()
        rcopy = pltpu.make_async_copy(r_hbm.at[pl.ds(base, per_level)], rs, rsem.at[0])
        dcopy = pltpu.make_async_copy(d_hbm.at[pl.ds(base, per_level)], ds, rsem.at[1])
        rcopy.start()
        dcopy.start()
        done = per_level * n_early
        ecopies = [
            pltpu.make_async_copy(e, o_ref.at[pl.ds(i * per_level, per_level)], esem.at[i])
            for i, e in enumerate(early)
        ]
        for c in ecopies:
            c.start()
        slots = []
        for s in range(total):
            b, k = divmod(s, slot_count)
            idx = table_ref[0 * total + s]
            lv = table_ref[1 * total + s]
            act = table_ref[2 * total + s]
            used = (act > 0) & (lv >= 0) & (lv < n_src)
            slots.append((used, b, k))
            for level in range(n_src):
                @pl.when((act > 0) & (lv == level))
                def _():
                    pltpu.make_async_copy(src[level].at[idx], xs.at[s], sem.at[s]).start()

            @pl.when(used)
            def _():
                pltpu.make_async_copy(f_hbm.at[base + b, k], fs.at[s], fsem.at[s]).start()

        for c in icopies:
            c.wait()
        for b in range(per_level):
            if n_init:
                acc[...] = ini[b]
            else:
                acc[...] = jnp.zeros_like(acc)
            for k in range(slot_count):
                s = b * slot_count + k
                used = slots[s][0]

                @pl.when(used)
                def _():
                    pltpu.make_async_copy(src[0].at[0], xs.at[s], sem.at[s]).wait()
                    pltpu.make_async_copy(f_hbm.at[0, 0], fs.at[s], fsem.at[s]).wait()
                    acc[...] += jnp.dot(fs[s], xs[s], preferred_element_type=jnp.float32)

            if b == 0:
                rcopy.wait()
                dcopy.wait()
                for c in ecopies:
                    c.wait()
            residual = (rs[b].astype(jnp.float32) - acc[...]).astype(jnp.bfloat16)
            o_ref[done + b] = jnp.dot(ds[b], residual, preferred_element_type=jnp.float32).astype(o_ref.dtype)

    any_spec = pl.BlockSpec(memory_space=pl.ANY)
    return pl.pallas_call(
        kernel,
        in_specs=[pl.BlockSpec(memory_space=pltpu.SMEM), any_spec, any_spec, any_spec]
        + [any_spec] * (n_src + n_early + n_init),
        out_specs=pl.BlockSpec(memory_space=pltpu.VMEM),
        scratch_shapes=[
            pltpu.VMEM((total, block, width), sources[0].dtype),
            pltpu.VMEM((total, block, block), factor.dtype),
            pltpu.VMEM((per_level, block, width), right.dtype),
            pltpu.VMEM((per_level, block, block), dinv.dtype),
            pltpu.VMEM((block, width), jnp.float32),
            pltpu.VMEM((per_level, block, width), jnp.float32),
            pltpu.SemaphoreType.DMA((total,)),
            pltpu.SemaphoreType.DMA((total,)),
            pltpu.SemaphoreType.DMA((3,)),
            pltpu.SemaphoreType.DMA((max(n_early, 1),)),
        ],
        out_shape=jax.ShapeDtypeStruct((per_level * (n_early + 1), block, width), jnp.bfloat16),
    )(table, factor, right, dinv, *sources, *earlier, *([] if init is None else [init]))


def partial_sum(table, factor, sources, slot_count, width, base, per_level):
    block = factor.shape[2]
    n_src = len(sources)
    total = per_level * slot_count

    def kernel(table_ref, f_hbm, *rest):
        src = rest[:n_src]
        o_ref, xs, fs, sem, fsem = rest[n_src:]
        slots = []
        for s in range(total):
            b, k = divmod(s, slot_count)
            idx = table_ref[0 * total + s]
            lv = table_ref[1 * total + s]
            act = table_ref[2 * total + s]
            used = (act > 0) & (lv >= 0) & (lv < n_src)
            slots.append(used)
            for level in range(n_src):
                @pl.when((act > 0) & (lv == level))
                def _():
                    pltpu.make_async_copy(src[level].at[idx], xs.at[s], sem.at[s]).start()

            @pl.when(used)
            def _():
                pltpu.make_async_copy(f_hbm.at[base + b, k], fs.at[s], fsem.at[s]).start()

        for b in range(per_level):
            o_ref[b] = jnp.zeros((block, width), jnp.float32)
            for k in range(slot_count):
                s = b * slot_count + k

                @pl.when(slots[s])
                def _():
                    pltpu.make_async_copy(src[0].at[0], xs.at[s], sem.at[s]).wait()
                    pltpu.make_async_copy(f_hbm.at[0, 0], fs.at[s], fsem.at[s]).wait()
                    o_ref[b] += jnp.dot(fs[s], xs[s], preferred_element_type=jnp.float32)

    any_spec = pl.BlockSpec(memory_space=pl.ANY)
    return pl.pallas_call(
        kernel,
        in_specs=[pl.BlockSpec(memory_space=pltpu.SMEM), any_spec] + [any_spec] * n_src,
        out_specs=pl.BlockSpec(memory_space=pltpu.VMEM),
        scratch_shapes=[
            pltpu.VMEM((total, block, width), sources[0].dtype),
            pltpu.VMEM((total, block, block), factor.dtype),
            pltpu.SemaphoreType.DMA((total,)),
            pltpu.SemaphoreType.DMA((total,)),
        ],
        out_shape=jax.ShapeDtypeStruct((per_level, block, width), jnp.float32),
    )(table, factor, *sources)


def shards(kernel_rows, factor_blocks, diag_inverse, pattern, live_counts):
    received = lax.all_to_all(kernel_rows, "rhs", split_axis=1, concat_axis=0, tiled=True)
    per_device = factor_blocks.shape[0]
    slot_count = factor_blocks.shape[1]
    block = factor_blocks.shape[2]
    width = received.shape[1]
    right_side = received.reshape(per_device, block, width)
    holders = lax.axis_size("rows")
    per_level = per_device // LEV
    level_of = pattern % per_device // per_level
    holder_of = pattern // per_device
    offset_of = pattern % per_level
    active = jnp.arange(slot_count)[None, :] < live_counts[:, None]
    position = jnp.clip(holder_of * per_level + offset_of, 0, holders * per_level - 1)
    gathered_all = []
    solved_all = []
    for level_now in range(LEV):
        lower = level_now * per_level
        upper = lower + per_level
        if level_now == 0:
            solved = jnp.einsum(
                "bij,bjr->bir", diag_inverse[lower:upper], right_side[lower:upper],
                preferred_element_type=jnp.float32,
            ).astype(jnp.bfloat16)
        else:
            newest = level_now - 1
            pos = position[lower:upper]
            lv = level_of[lower:upper]
            act = active[lower:upper].astype(jnp.int32)
            init = None
            if newest > 0:
                old_table = jnp.stack([pos, lv, act]).reshape(-1).astype(jnp.int32)
                init = partial_sum(
                    old_table, factor_blocks, gathered_all[:newest], slot_count, width, lower, per_level
                )
            table = jnp.stack([pos, jnp.where(lv == newest, 0, -1), act]).reshape(-1).astype(jnp.int32)
            solved = level_solve(
                table,
                factor_blocks,
                right_side,
                diag_inverse,
                gathered_all[newest:],
                slot_count,
                lower,
                per_level,
                earlier=tuple(solved_all) if level_now + 1 == LEV else (),
                init=init,
            )
        if level_now + 1 < LEV:
            solved_all.append(solved)
            gathered_all.append(lax.all_gather(solved, "rows", axis=0, tiled=True))
    return solved.reshape(per_device * block, width)


def solution(mesh):
    placed = (
        P(("rows", "rhs"), None),
        P("rows", None, None, None),
        P("rows", None, None),
        P("rows", None),
        P("rows"),
    )
    return jax.shard_map(
        shards, mesh=mesh, in_specs=placed, out_specs=P("rows", "rhs"), check_vma=False
    )
```
